256 devices in a mesh: ctx: 4 (over x_hi, core), exp: 64 (over y, z, x_lo).
Axes of the slice: x: 4 (x_hi: 2, x_lo: 2; x = x_hi * 2 + x_lo), y: 4, z: 8, core: 2. Of those that a mesh axis runs over, the one named last changes fastest.
Arguments:
- queries: bfloat16 [64, 1024, 2048], P('exp', 'ctx'), may hold values from -5 to 5
- key_rows: bfloat16 [64, 1024, 2048], P('exp', 'ctx'), may hold values from -5 to 5
- value_rows: bfloat16 [64, 1024, 2048], P('exp', 'ctx'), may hold values from -6 to 6
- residual_in: bfloat16 [64, 1024, 2048], P('exp', 'ctx'), may hold values from -6 to 6
- norm_gain: float32 [2048], replicated, may hold values from 0.1 to 1.9
- routes: int32 [64, 1024, 2], P('exp', 'ctx'), may hold values from 0 to 63, all different within a row; in each aligned block of 256 rows (0 to 255, 256 to 511, ..., all dimensions but the last counted through in order) at most 10 rows name the same one
- gate_weights: float32 [64, 1024, 2], P('exp', 'ctx'), may hold values from 0.25 to 1
- gate_up_weight: bfloat16 [64, 2048, 2, 1024], P('exp', None, None, 'ctx'), may hold values from -0.125 to 0.125
- down_weight: bfloat16 [64, 1024, 2048], P('exp', 'ctx'), may hold values from -0.1875 to 0.1875
Outputs:
- layer_out: bfloat16 [64, 1024, 2048], P('exp', 'ctx')
The draws below stay inside these ranges and needn't reach their ends.
Inputs may be any that keep to these rules, and one draw needn't show every extreme that they name: `routes`: within the rows of one device (aligned blocks of 256 tokens in clip-then-frame order), no expert is named more than 10 times; the 2 experts of a token differ.
All inputs are finite; a program needn't handle non-finite values.
Results may differ from the reference program's by a relative error of at most 0.011.
Values may be sent and summed in bfloat16 or wider, within the bound.
No kernel may reach another device: no remote copies, remote signals or barrier semaphores. Data moves between devices by JAX's collectives and lax.ppermute only.
A program may use at most 128 MiB of HBM per device.

```python
import math
import jax
import jax.numpy as jnp
import numpy as np
from jax import lax

HEADS = 16
HEAD = 128
D = 2048
FF = 1024
TOP = 2
TOK_DEV = 256
LEN = 1024
CLIPS = 64
EXPERTS = 64
CAP = 10
TOKENS = 65536
N_CTX = 4
N_EXP = 64


def draw_queries(key, part):
    result = jax.random.truncated_normal(jax.random.fold_in(key, 1), -5.0, 5.0, (CLIPS, LEN, D), jnp.float32)
    return result.astype(jnp.bfloat16)


def draw_key_rows(key, part):
    result = jax.random.truncated_normal(jax.random.fold_in(key, 2), -5.0, 5.0, (CLIPS, LEN, D), jnp.float32)
    return result.astype(jnp.bfloat16)


def level_of(key, extent, pieces, smallest, top_value):
    level = 1.0
    for dim, shards_of in pieces:
        draws = jax.random.uniform(jax.random.fold_in(jax.random.fold_in(key, 6), dim), (shards_of,), jnp.float32, smallest / len(pieces), top_value / len(pieces))
        level = level * jnp.repeat(jnp.exp(draws), extent[dim] // shards_of).reshape((-1,) + (1,) * (len(extent) - 1 - dim))
    return level


def shared_out(rng, own, number, rows, amount, top, limit, lean):
    order = jax.random.permutation(rng, amount)
    crowded, usual = portions_of(amount, rows * top, limit, lean, True), portions_of(amount, rows * top, limit, lean, False)
    places = jnp.arange(amount)

    def named(tallies, turn):
        used = int((tallies > 0).sum())
        fixed = max(1, used // 4)
        shifted = fixed + (places - fixed + turn * (used - fixed)) % max(1, amount - fixed)
        return jnp.zeros((amount,), jnp.int32).at[order[jnp.where(places < fixed, places, shifted)]].set(jnp.asarray(tallies, jnp.int32))

    tallies = jnp.where(number % 4 == 0, named(crowded, number // 4), named(usual, number - number // 4 - 1))
    mixed = jax.random.permutation(jax.random.fold_in(own, 3), amount)
    source_of, receiver = mixed[0:amount // 2 * 2:2], mixed[1:amount // 2 * 2:2]
    room = jnp.minimum(tallies[source_of] - 1, limit - tallies[receiver]) // 2
    room = jnp.where((source_of == order[0]) | (receiver == order[0]) | (tallies[receiver] == 0), 0, jnp.maximum(room, 0))
    shifted = jax.random.randint(jax.random.fold_in(own, 4), (amount // 2,), 0, 1 << 20) % (room + 1)
    tallies = tallies.at[source_of].add(-shifted).at[receiver].add(shifted)
    items = jnp.searchsorted(jnp.cumsum(tallies), jnp.arange(rows * top), side="right").astype(jnp.int32)
    grid = items.reshape(top, rows).T
    grid = grid[jax.random.permutation(jax.random.fold_in(own, 1), rows)]
    turn = jax.random.randint(jax.random.fold_in(own, 2), (rows, 1), 0, top)
    return jnp.take_along_axis(grid, (jnp.arange(top)[None, :] + turn) % top, axis=1)


def portions_of(number_of, total, limit, lean, full):
    loads = [(1 << 20) // math.isqrt(rank ** lean) + 1 for rank in range(1, number_of + 1)]
    largest = limit if full else min(limit, max(-(-total // number_of), total * loads[0] // sum(loads)))
    least = 1 if total - largest >= number_of - 1 else 0
    counts, surplus = [largest] + [least] * (number_of - 1), total - largest - least * (number_of - 1)
    while surplus > 0:
        free = [i for i in range(1, number_of) if counts[i] < largest] or [i for i in range(1, number_of) if counts[i] < limit]
        mass, left = sum([loads[i] for i in free]), surplus
        for i in free:
            more = min(limit - counts[i], max(1, left * loads[i] // mass), surplus)
            counts[i] = counts[i] + more
            surplus = surplus - more
    return np.array(counts)


def scatter_about(rng, dims, deviation, most, cuts=(), kind=jnp.bfloat16):
    gain = level_of(rng, dims, cuts, -0.22, 0.18) if cuts else 1.0
    drawn = jax.random.normal(rng, dims, jnp.float32) * deviation * gain
    return jnp.minimum(jnp.maximum(drawn, -most), most).astype(kind)


def setup_inputs(seed: int = 0) -> dict:
    keys = jax.random.split(jax.random.key(seed), 10)
    queries = draw_queries(jax.random.fold_in(keys[9], 71), 0)
    key_rows = draw_key_rows(jax.random.fold_in(keys[9], 71), 0)
    value_rows = scatter_about(keys[2], (CLIPS, LEN, D), 1.0, 6.0, ((0, 64), (1, 4)))
    residual_in = scatter_about(keys[3], (CLIPS, LEN, D), 1.0, 6.0, ((0, 64), (1, 4)))
    norm_gain = jnp.clip(1.0 + 0.18 * jax.random.normal(keys[4], (D,), jnp.float32), 0.1, 1.9)
    routes_keys = jax.random.split(jax.random.fold_in(keys[5], 1), CLIPS * LEN // TOK_DEV)
    routes_turns = jax.random.permutation(jax.random.fold_in(keys[5], 3), CLIPS * LEN // TOK_DEV)
    routes = jax.vmap(lambda own, number: shared_out(jax.random.fold_in(keys[5], 2), own, number, TOK_DEV, EXPERTS, TOP, CAP, 2))(routes_keys, routes_turns).reshape((CLIPS, LEN, TOP))
    gate_weights = jnp.clip(0.25 + 0.75 * jax.random.uniform(keys[6], (CLIPS, LEN, TOP), jnp.float32) ** level_of(keys[6], (CLIPS, LEN, TOP), ((0, 64), (1, 4)), -0.2, 0.2), 0.25, 1.0)
    gate_up_weight = scatter_about(keys[7], (EXPERTS, D, 2, FF), D ** -0.5, 0.125, ((0, 64), (3, 4)))
    down_weight = scatter_about(keys[8], (EXPERTS, FF, D), FF ** -0.5, 0.1875, ((0, 64), (1, 4)))
    return {"queries": queries, "key_rows": key_rows, "value_rows": value_rows, "residual_in": residual_in, "norm_gain": norm_gain, "routes": routes, "gate_weights": gate_weights, "gate_up_weight": gate_up_weight, "down_weight": down_weight}


def clip_attention(operands):
    query_part, key_part, value_part = operands
    query_heads = query_part.reshape(LEN, HEADS, HEAD).astype(jnp.float32)
    key_heads = key_part.reshape(LEN, HEADS, HEAD).astype(jnp.float32)
    value_heads = value_part.reshape(LEN, HEADS, HEAD).astype(jnp.float32)
    scores = jnp.einsum('qhd,khd->qhk', query_heads, key_heads) * HEAD ** (-0.5)
    row_max = lax.optimization_barrier(jnp.max(scores, axis=-1, keepdims=True))
    expo = jnp.exp(scores - row_max)
    row_total = lax.optimization_barrier(jnp.sum(expo, axis=-1))
    probs = lax.optimization_barrier(expo.astype(jnp.bfloat16)).astype(jnp.float32)
    weighted = jnp.einsum('qhk,khd->qhd', probs, value_heads)
    return (weighted / row_total[..., None]).reshape(LEN, D)

def reference(queries, key_rows, value_rows, residual_in, norm_gain, routes, gate_weights, gate_up_weight, down_weight):
    attention = lax.map(clip_attention, (queries, key_rows, value_rows))
    mixed_rows = (residual_in.astype(jnp.float32) + attention).astype(jnp.bfloat16)
    mixed_float = mixed_rows.astype(jnp.float32)
    mean_square = lax.optimization_barrier(jnp.mean(mixed_float * mixed_float, axis=-1, keepdims=True))
    normed = (mixed_float * lax.rsqrt(mean_square + 1e-05) * norm_gain).astype(jnp.bfloat16)
    flat_normed = normed.reshape(TOKENS, D)
    flat_routes = routes.reshape(TOKENS, TOP)
    flat_gates = gate_weights.reshape(TOKENS, TOP)
    max_rows = min(N_CTX * N_EXP * CAP, TOKENS)
    group_width = FF // N_CTX

    def one_expert(accumulated, expert_id):
        is_routed = flat_routes == expert_id
        weight = lax.optimization_barrier(jnp.sum(jnp.where(is_routed, flat_gates, 0.0), axis=1))
        sort_key = jnp.where(jnp.any(is_routed, axis=1), 0, 1).astype(jnp.int32)
        row_order = jnp.argsort(sort_key, stable=True)[:max_rows].astype(jnp.int32)
        picked = flat_normed[row_order]
        gate_and_up = jnp.dot(picked, gate_up_weight[expert_id].reshape(D, 2 * FF), preferred_element_type=jnp.float32)
        hidden = (jax.nn.silu(gate_and_up[:, :FF]) * gate_and_up[:, FF:]).astype(jnp.bfloat16)
        group_parts = jnp.einsum('rgf,gfd->grd', hidden.reshape(max_rows, N_CTX, group_width).astype(jnp.float32), down_weight[expert_id].reshape(N_CTX, group_width, D).astype(jnp.float32))
        group_parts = lax.optimization_barrier(group_parts.astype(jnp.bfloat16)).astype(jnp.float32)
        expert_out = lax.optimization_barrier(jnp.sum(group_parts, axis=0)).astype(jnp.bfloat16).astype(jnp.float32)
        accumulated = accumulated.at[row_order].add(weight[row_order][:, None] * expert_out)
        return (accumulated, None)
    expert_sum, _ = lax.scan(one_expert, jnp.zeros((TOKENS, D), jnp.float32), jnp.arange(EXPERTS, dtype=jnp.int32))
    result = (mixed_float.reshape(TOKENS, D) + expert_sum).astype(jnp.bfloat16)
    return result.reshape(CLIPS, LEN, D)
```

```python
import jax
import jax.numpy as jnp
from jax import lax
from jax.sharding import PartitionSpec as P

HEADS = 16


def shards(
    queries,
    key_rows,
    value_rows,
    residual_in,
    norm_gain,
    routes,
    gate_weights,
    gate_up_weight,
    down_weight,
):
    clip_count, row_count, feature_count = queries.shape
    head_count = HEADS
    head_size = feature_count // head_count
    score_scale = head_size ** (-0.5)
    query_heads = queries.reshape(clip_count, row_count, head_count, head_size)
    running_max = jnp.full((clip_count, row_count, head_count), -1e30, jnp.float32)
    key_part = lax.all_gather(key_rows, "ctx", axis=1, tiled=True)
    value_part = lax.all_gather(value_rows, "ctx", axis=1, tiled=True)
    key_heads = key_part.reshape(clip_count, -1, head_count, head_size)
    value_heads = value_part.reshape(clip_count, -1, head_count, head_size)
    scores = (
        jnp.einsum("cqhd,ckhd->cqhk", query_heads, key_heads, preferred_element_type=jnp.float32)
        * score_scale
    )
    new_max = jnp.maximum(running_max, jnp.max(scores, axis=-1))
    expo = jnp.exp(scores - new_max[..., None])
    running_sum = jnp.sum(expo, axis=-1)
    weighted = jnp.einsum(
        "cqhk,ckhd->cqhd",
        expo.astype(jnp.bfloat16),
        value_heads,
        preferred_element_type=jnp.float32,
    )
    final_max, final_sum, weighted = (new_max, running_sum, weighted)
    attention = (weighted / final_sum[..., None]).reshape(clip_count, row_count, feature_count)
    mixed_rows = (residual_in.astype(jnp.float32) + attention).astype(jnp.bfloat16)
    mixed_float = mixed_rows.astype(jnp.float32)
    mean_square = jnp.mean(mixed_float * mixed_float, axis=-1, keepdims=True)
    normed = (mixed_float * lax.rsqrt(mean_square + 1e-05) * norm_gain).astype(jnp.bfloat16)
    token_count = clip_count * row_count
    top_count = routes.shape[-1]
    expert_count = lax.axis_size("exp") * gate_up_weight.shape[0]
    capacity = max(2, -(-(5 * token_count * top_count) // (4 * expert_count)))
    flat_routes = routes.reshape(-1)
    one_hot = (flat_routes[:, None] == jnp.arange(expert_count, dtype=jnp.int32)[None, :]).astype(
        jnp.int32
    )
    running_count = jnp.cumsum(one_hot, axis=0)
    slot_index = jnp.sum(running_count * one_hot, axis=1) - 1
    destination = flat_routes * capacity + slot_index
    source_rows = jnp.repeat(normed.reshape(token_count, feature_count), top_count, axis=0)
    send_buffer = (
        jnp.zeros((expert_count * capacity, feature_count), jnp.bfloat16)
        .at[destination]
        .set(source_rows)
    )
    send_buffer = send_buffer.reshape(expert_count, capacity, feature_count)
    full_gate_up = lax.all_gather(gate_up_weight[0], "ctx", axis=2, tiled=True)
    full_down = lax.all_gather(down_weight[0], "ctx", axis=0, tiled=True)
    unit_count = full_down.shape[0]
    group_count = lax.axis_size("ctx")
    group_width = unit_count // group_count
    portion = lax.all_to_all(send_buffer, "exp", split_axis=0, concat_axis=0, tiled=True)
    flattened = portion.reshape(-1, feature_count)
    gate_and_up = jnp.dot(
        flattened,
        full_gate_up.reshape(feature_count, 2 * unit_count),
        preferred_element_type=jnp.float32,
    )
    hidden = (jax.nn.silu(gate_and_up[:, :unit_count]) * gate_and_up[:, unit_count:]).astype(
        jnp.bfloat16
    )
    group_parts = jnp.einsum(
        "rgf,gfd->grd",
        hidden.reshape(-1, group_count, group_width),
        full_down.reshape(group_count, group_width, feature_count),
        preferred_element_type=jnp.float32,
    ).astype(jnp.bfloat16)
    summed = jnp.sum(group_parts.astype(jnp.float32), axis=0).astype(jnp.bfloat16)
    summed = summed.reshape(portion.shape)
    returned = lax.all_to_all(summed, "exp", split_axis=0, concat_axis=0, tiled=True)
    expert_out = returned.reshape(-1, feature_count)[destination]
    expert_out = expert_out.reshape(token_count, top_count, feature_count).astype(jnp.float32)
    expert_sum = jnp.sum(gate_weights.reshape(token_count, top_count, 1) * expert_out, axis=1)
    layer_out = (mixed_float.reshape(token_count, feature_count) + expert_sum).astype(jnp.bfloat16)
    return layer_out.reshape(clip_count, row_count, feature_count)


def solution(mesh):
    return jax.shard_map(
        shards,
        mesh=mesh,
        in_specs=(
            P("exp", "ctx", None),
            P("exp", "ctx", None),
            P("exp", "ctx", None),
            P("exp", "ctx", None),
            P(),
            P("exp", "ctx", None),
            P("exp", "ctx", None),
            P("exp", None, None, "ctx"),
            P("exp", "ctx", None),
        ),
        out_specs=P("exp", "ctx", None),
        check_vma=False,
    )
```

```python
import jax
import jax.numpy as jnp
from jax import lax
from jax.sharding import PartitionSpec as P

HEADS = 16


def ctx_blocks(block):
    count = lax.axis_size("ctx")
    if count != 4:
        gathered = lax.all_gather(block, "ctx", axis=0)
        return [gathered[i] for i in range(count)]
    far = lax.ppermute(block, "ctx", perm=[(c, c ^ 2) for c in range(count)])
    near = lax.ppermute(jnp.stack([block, far]), "ctx", perm=[(c, c ^ 1) for c in range(count)])
    return [block, far, near[0], near[1]]


def shards(
    queries,
    key_rows,
    value_rows,
    residual_in,
    norm_gain,
    routes,
    gate_weights,
    gate_up_weight,
    down_weight,
):
    clip_count, row_count, feature_count = queries.shape
    head_count = HEADS
    head_size = feature_count // head_count
    score_scale = head_size ** (-0.5)
    query_heads = queries.reshape(clip_count, row_count, head_count, head_size)
    running_max = jnp.full((clip_count, row_count, head_count), -1e30, jnp.float32)
    key_part = jnp.concatenate(ctx_blocks(key_rows), axis=1)
    value_part = jnp.concatenate(ctx_blocks(value_rows), axis=1)
    key_heads = key_part.reshape(clip_count, -1, head_count, head_size)
    value_heads = value_part.reshape(clip_count, -1, head_count, head_size)
    scores = (
        jnp.einsum("cqhd,ckhd->cqhk", query_heads, key_heads, preferred_element_type=jnp.float32)
        * score_scale
    )
    new_max = jnp.maximum(running_max, jnp.max(scores, axis=-1))
    expo = jnp.exp(scores - new_max[..., None])
    running_sum = jnp.sum(expo, axis=-1)
    weighted = jnp.einsum(
        "cqhk,ckhd->cqhd",
        expo.astype(jnp.bfloat16),
        value_heads,
        preferred_element_type=jnp.float32,
    )
    final_max, final_sum, weighted = (new_max, running_sum, weighted)
    attention = (weighted / final_sum[..., None]).reshape(clip_count, row_count, feature_count)
    mixed_rows = (residual_in.astype(jnp.float32) + attention).astype(jnp.bfloat16)
    mixed_float = mixed_rows.astype(jnp.float32)
    mean_square = jnp.mean(mixed_float * mixed_float, axis=-1, keepdims=True)
    normed = (mixed_float * lax.rsqrt(mean_square + 1e-05) * norm_gain).astype(jnp.bfloat16)
    token_count = clip_count * row_count
    top_count = routes.shape[-1]
    expert_count = lax.axis_size("exp") * gate_up_weight.shape[0]
    capacity = max(2, -(-(5 * token_count * top_count) // (4 * expert_count)))
    flat_routes = routes.reshape(-1)
    one_hot = (flat_routes[:, None] == jnp.arange(expert_count, dtype=jnp.int32)[None, :]).astype(
        jnp.int32
    )
    running_count = jnp.cumsum(one_hot, axis=0)
    slot_index = jnp.sum(running_count * one_hot, axis=1) - 1
    destination = flat_routes * capacity + slot_index
    slot_token = (
        jnp.zeros((expert_count * capacity,), jnp.int32)
        .at[destination]
        .set(jnp.arange(token_count * top_count, dtype=jnp.int32) // top_count)
    )
    send_buffer = normed.reshape(token_count, feature_count)[slot_token]
    send_buffer = send_buffer.reshape(expert_count, capacity, feature_count)
    local_units = down_weight.shape[1]
    gate_up_blocks = ctx_blocks(gate_up_weight[0].reshape(feature_count, 2 * local_units))
    down_blocks = ctx_blocks(down_weight[0])
    portion = lax.all_to_all(send_buffer, "exp", split_axis=0, concat_axis=0, tiled=True)
    flattened = portion.reshape(-1, feature_count)
    summed = None
    for gate_up_block, down_block in zip(gate_up_blocks, down_blocks):
        gate_and_up = jnp.dot(flattened, gate_up_block, preferred_element_type=jnp.float32)
        hidden = (
            jax.nn.silu(gate_and_up[:, :local_units]) * gate_and_up[:, local_units:]
        ).astype(jnp.bfloat16)
        group_part = jnp.dot(hidden, down_block, preferred_element_type=jnp.float32)
        group_part = group_part.astype(jnp.bfloat16).astype(jnp.float32)
        summed = group_part if summed is None else summed + group_part
    summed = summed.astype(jnp.bfloat16).reshape(portion.shape)
    returned = lax.all_to_all(summed, "exp", split_axis=0, concat_axis=0, tiled=True)
    expert_out = returned.reshape(-1, feature_count)[destination]
    expert_out = expert_out.reshape(token_count, top_count, feature_count).astype(jnp.float32)
    expert_sum = jnp.sum(gate_weights.reshape(token_count, top_count, 1) * expert_out, axis=1)
    layer_out = (mixed_float.reshape(token_count, feature_count) + expert_sum).astype(jnp.bfloat16)
    return layer_out.reshape(clip_count, row_count, feature_count)


def solution(mesh):
    return jax.shard_map(
        shards,
        mesh=mesh,
        in_specs=(
            P("exp", "ctx", None),
            P("exp", "ctx", None),
            P("exp", "ctx", None),
            P("exp", "ctx", None),
            P(),
            P("exp", "ctx", None),
            P("exp", "ctx", None),
            P("exp", None, None, "ctx"),
            P("exp", "ctx", None),
        ),
        out_specs=P("exp", "ctx", None),
        check_vma=False,
    )
```

```python
import jax
import jax.numpy as jnp
from jax import lax
from jax.sharding import PartitionSpec as P

HEADS = 16


def far_block(block, after=None):
    if after is not None:
        block, _ = lax.optimization_barrier((block, after))
    return lax.ppermute(block, "ctx", perm=[(c, c ^ 2) for c in range(4)])


def near_blocks(block, far):
    near = lax.ppermute(jnp.stack([block, far]), "ctx", perm=[(c, c ^ 1) for c in range(4)])
    return [block, far, near[0], near[1]]


def shards(
    queries,
    key_rows,
    value_rows,
    residual_in,
    norm_gain,
    routes,
    gate_weights,
    gate_up_weight,
    down_weight,
):
    clip_count, row_count, feature_count = queries.shape
    head_count = HEADS
    head_size = feature_count // head_count
    score_scale = head_size ** (-0.5)
    query_heads = queries.reshape(clip_count, row_count, head_count, head_size)
    running_max = jnp.full((clip_count, row_count, head_count), -1e30, jnp.float32)
    local_units = down_weight.shape[1]
    gate_up_local = gate_up_weight[0].reshape(feature_count, 2 * local_units)
    down_local = down_weight[0]
    key_far = far_block(key_rows)
    value_far = far_block(value_rows, key_far)
    gate_up_far = far_block(gate_up_local, value_far)
    down_far = far_block(down_local, gate_up_far)
    key_part = jnp.concatenate(near_blocks(key_rows, key_far), axis=1)
    value_part = jnp.concatenate(near_blocks(value_rows, value_far), axis=1)
    key_heads = key_part.reshape(clip_count, -1, head_count, head_size)
    value_heads = value_part.reshape(clip_count, -1, head_count, head_size)
    scores = (
        jnp.einsum("cqhd,ckhd->cqhk", query_heads, key_heads, preferred_element_type=jnp.float32)
        * score_scale
    )
    new_max = jnp.maximum(running_max, jnp.max(scores, axis=-1))
    expo = jnp.exp(scores - new_max[..., None])
    running_sum = jnp.sum(expo, axis=-1)
    weighted = jnp.einsum(
        "cqhk,ckhd->cqhd",
        expo.astype(jnp.bfloat16),
        value_heads,
        preferred_element_type=jnp.float32,
    )
    final_max, final_sum, weighted = (new_max, running_sum, weighted)
    attention = (weighted / final_sum[..., None]).reshape(clip_count, row_count, feature_count)
    mixed_rows = (residual_in.astype(jnp.float32) + attention).astype(jnp.bfloat16)
    mixed_float = mixed_rows.astype(jnp.float32)
    mean_square = jnp.mean(mixed_float * mixed_float, axis=-1, keepdims=True)
    normed = (mixed_float * lax.rsqrt(mean_square + 1e-05) * norm_gain).astype(jnp.bfloat16)
    token_count = clip_count * row_count
    top_count = routes.shape[-1]
    expert_count = lax.axis_size("exp") * gate_up_weight.shape[0]
    capacity = max(2, -(-(5 * token_count * top_count) // (4 * expert_count)))
    flat_routes = routes.reshape(-1)
    one_hot = (flat_routes[:, None] == jnp.arange(expert_count, dtype=jnp.int32)[None, :]).astype(
        jnp.int32
    )
    running_count = jnp.cumsum(one_hot, axis=0)
    slot_index = jnp.sum(running_count * one_hot, axis=1) - 1
    destination = flat_routes * capacity + slot_index
    slot_token = (
        jnp.zeros((expert_count * capacity,), jnp.int32)
        .at[destination]
        .set(jnp.arange(token_count * top_count, dtype=jnp.int32) // top_count)
    )
    normed, gate_up_far, down_far = lax.optimization_barrier((normed, gate_up_far, down_far))
    send_buffer = normed.reshape(token_count, feature_count)[slot_token]
    send_buffer = send_buffer.reshape(expert_count, capacity * feature_count)
    gate_up_blocks = near_blocks(gate_up_local, gate_up_far)
    down_blocks = near_blocks(down_local, down_far)
    portion = lax.all_to_all(send_buffer, "exp", split_axis=0, concat_axis=0, tiled=True)
    flattened = portion.reshape(-1, feature_count)
    summed = None
    for gate_up_block, down_block in zip(gate_up_blocks, down_blocks):
        gate_and_up = jnp.dot(flattened, gate_up_block, preferred_element_type=jnp.float32)
        hidden = (
            jax.nn.silu(gate_and_up[:, :local_units]) * gate_and_up[:, local_units:]
        ).astype(jnp.bfloat16)
        group_part = jnp.dot(hidden, down_block, preferred_element_type=jnp.float32)
        group_part = group_part.astype(jnp.bfloat16).astype(jnp.float32)
        summed = group_part if summed is None else summed + group_part
    summed = summed.astype(jnp.bfloat16).reshape(portion.shape)
    returned = lax.all_to_all(summed, "exp", split_axis=0, concat_axis=0, tiled=True)
    expert_out = returned.reshape(-1, feature_count)[destination]
    expert_out = expert_out.reshape(token_count, top_count, feature_count).astype(jnp.float32)
    expert_sum = jnp.sum(gate_weights.reshape(token_count, top_count, 1) * expert_out, axis=1)
    layer_out = (mixed_float.reshape(token_count, feature_count) + expert_sum).astype(jnp.bfloat16)
    return layer_out.reshape(clip_count, row_count, feature_count)


def solution(mesh):
    return jax.shard_map(
        shards,
        mesh=mesh,
        in_specs=(
            P("exp", "ctx", None),
            P("exp", "ctx", None),
            P("exp", "ctx", None),
            P("exp", "ctx", None),
            P(),
            P("exp", "ctx", None),
            P("exp", "ctx", None),
            P("exp", None, None, "ctx"),
            P("exp", "ctx", None),
        ),
        out_specs=P("exp", "ctx", None),
        check_vma=False,
    )
```

```python
import jax
import jax.numpy as jnp
from jax import lax
from jax.sharding import PartitionSpec as P

HEADS = 16


def far_block(block, after=None):
    if after is not None:
        block, _ = lax.optimization_barrier((block, after))
    return lax.ppermute(block, "ctx", perm=[(c, c ^ 2) for c in range(4)])


def near_blocks(block, far):
    near = lax.ppermute(jnp.stack([block, far]), "ctx", perm=[(c, c ^ 1) for c in range(4)])
    return [block, far, near[0], near[1]]


def shards(
    queries,
    key_rows,
    value_rows,
    residual_in,
    norm_gain,
    routes,
    gate_weights,
    gate_up_weight,
    down_weight,
):
    clip_count, row_count, feature_count = queries.shape
    head_count = HEADS
    head_size = feature_count // head_count
    score_scale = head_size ** (-0.5)
    query_heads = queries.reshape(clip_count, row_count, head_count, head_size)
    running_max = jnp.full((clip_count, row_count, head_count), -1e30, jnp.float32)
    local_units = down_weight.shape[1]
    gate_up_local = gate_up_weight[0].reshape(feature_count, 2 * local_units)
    down_local = down_weight[0]
    key_far = far_block(key_rows)
    value_far = far_block(value_rows, key_far)
    gate_up_far = far_block(gate_up_local, value_far)
    down_far = far_block(down_local, gate_up_far)
    key_part = jnp.concatenate(near_blocks(key_rows, key_far), axis=1)
    value_part = jnp.concatenate(near_blocks(value_rows, value_far), axis=1)
    key_heads = key_part.reshape(clip_count, -1, head_count, head_size)
    value_heads = value_part.reshape(clip_count, -1, head_count, head_size)
    scores = (
        jnp.einsum("cqhd,ckhd->cqhk", query_heads, key_heads, preferred_element_type=jnp.float32)
        * score_scale
    )
    new_max = jnp.maximum(running_max, jnp.max(scores, axis=-1))
    expo = jnp.exp(scores - new_max[..., None])
    running_sum = jnp.sum(expo, axis=-1)
    weighted = jnp.einsum(
        "cqhk,ckhd->cqhd",
        expo.astype(jnp.bfloat16),
        value_heads,
        preferred_element_type=jnp.float32,
    )
    final_max, final_sum, weighted = (new_max, running_sum, weighted)
    attention = (weighted / final_sum[..., None]).reshape(clip_count, row_count, feature_count)
    mixed_rows = (residual_in.astype(jnp.float32) + attention).astype(jnp.bfloat16)
    mixed_float = mixed_rows.astype(jnp.float32)
    mean_square = jnp.mean(mixed_float * mixed_float, axis=-1, keepdims=True)
    normed = (mixed_float * lax.rsqrt(mean_square + 1e-05) * norm_gain).astype(jnp.bfloat16)
    token_count = clip_count * row_count
    top_count = routes.shape[-1]
    expert_count = lax.axis_size("exp") * gate_up_weight.shape[0]
    capacity = max(2, -(-(5 * token_count * top_count) // (4 * expert_count)))
    flat_routes = routes.reshape(-1)
    one_hot = (flat_routes[:, None] == jnp.arange(expert_count, dtype=jnp.int32)[None, :]).astype(
        jnp.int32
    )
    running_count = jnp.cumsum(one_hot, axis=0)
    slot_index = jnp.sum(running_count * one_hot, axis=1) - 1
    destination = flat_routes * capacity + slot_index
    slot_token = (
        jnp.zeros((expert_count * capacity,), jnp.int32)
        .at[destination]
        .set(jnp.arange(token_count * top_count, dtype=jnp.int32) // top_count)
    )
    normed, gate_up_far = lax.optimization_barrier((normed, gate_up_far))
    send_buffer = normed.reshape(token_count, feature_count)[slot_token]
    send_buffer = send_buffer.reshape(expert_count, capacity * 8, feature_count // 8)
    gate_up_blocks = near_blocks(gate_up_local, gate_up_far)
    down_blocks = near_blocks(down_local, down_far)
    portion = lax.all_to_all(send_buffer, "exp", split_axis=0, concat_axis=0, tiled=True)
    flattened = portion.reshape(-1, feature_count)
    summed = None
    for gate_up_block, down_block in zip(gate_up_blocks, down_blocks):
        gate_and_up = jnp.dot(flattened, gate_up_block, preferred_element_type=jnp.float32)
        hidden = (
            jax.nn.silu(gate_and_up[:, :local_units]) * gate_and_up[:, local_units:]
        ).astype(jnp.bfloat16)
        group_part = jnp.dot(hidden, down_block, preferred_element_type=jnp.float32)
        group_part = group_part.astype(jnp.bfloat16).astype(jnp.float32)
        summed = group_part if summed is None else summed + group_part
    summed = summed.astype(jnp.bfloat16).reshape(portion.shape)
    returned = lax.all_to_all(summed, "exp", split_axis=0, concat_axis=0, tiled=True)
    expert_out = returned.reshape(-1, feature_count)[destination]
    expert_out = expert_out.reshape(token_count, top_count, feature_count).astype(jnp.float32)
    expert_sum = jnp.sum(gate_weights.reshape(token_count, top_count, 1) * expert_out, axis=1)
    layer_out = (mixed_float.reshape(token_count, feature_count) + expert_sum).astype(jnp.bfloat16)
    return layer_out.reshape(clip_count, row_count, feature_count)


def solution(mesh):
    return jax.shard_map(
        shards,
        mesh=mesh,
        in_specs=(
            P("exp", "ctx", None),
            P("exp", "ctx", None),
            P("exp", "ctx", None),
            P("exp", "ctx", None),
            P(),
            P("exp", "ctx", None),
            P("exp", "ctx", None),
            P("exp", None, None, "ctx"),
            P("exp", "ctx", None),
        ),
        out_specs=P("exp", "ctx", None),
        check_vma=False,
    )
```

```python
import jax
import jax.numpy as jnp
from jax import lax
from jax.sharding import PartitionSpec as P

HEADS = 16


def far_block(block, after=None):
    if after is not None:
        block, _ = lax.optimization_barrier((block, after))
    return lax.ppermute(block, "ctx", perm=[(c, c ^ 2) for c in range(4)])


def near_blocks(block, far):
    perm = [(c, c ^ 1) for c in range(4)]
    return [block, far, lax.ppermute(block, "ctx", perm=perm), lax.ppermute(far, "ctx", perm=perm)]


def shards(
    queries,
    key_rows,
    value_rows,
    residual_in,
    norm_gain,
    routes,
    gate_weights,
    gate_up_weight,
    down_weight,
):
    clip_count, row_count, feature_count = queries.shape
    head_count = HEADS
    head_size = feature_count // head_count
    score_scale = head_size ** (-0.5)
    query_heads = queries.reshape(clip_count, row_count, head_count, head_size)
    running_max = jnp.full((clip_count, row_count, head_count), -1e30, jnp.float32)
    local_units = down_weight.shape[1]
    gate_up_local = gate_up_weight[0].reshape(feature_count, 2 * local_units)
    down_local = down_weight[0]
    key_far = far_block(key_rows)
    value_far = far_block(value_rows, key_far)
    gate_up_far = far_block(gate_up_local, value_far)
    down_far = far_block(down_local, gate_up_far)
    key_part = jnp.concatenate(near_blocks(key_rows, key_far), axis=1)
    value_part = jnp.concatenate(near_blocks(value_rows, value_far), axis=1)
    key_heads = key_part.reshape(clip_count, -1, head_count, head_size)
    value_heads = value_part.reshape(clip_count, -1, head_count, head_size)
    scores = (
        jnp.einsum("cqhd,ckhd->cqhk", query_heads, key_heads, preferred_element_type=jnp.float32)
        * score_scale
    )
    new_max = jnp.maximum(running_max, jnp.max(scores, axis=-1))
    expo = jnp.exp(scores - new_max[..., None])
    running_sum = jnp.sum(expo, axis=-1)
    weighted = jnp.einsum(
        "cqhk,ckhd->cqhd",
        expo.astype(jnp.bfloat16),
        value_heads,
        preferred_element_type=jnp.float32,
    )
    final_max, final_sum, weighted = (new_max, running_sum, weighted)
    attention = (weighted / final_sum[..., None]).reshape(clip_count, row_count, feature_count)
    mixed_rows = (residual_in.astype(jnp.float32) + attention).astype(jnp.bfloat16)
    mixed_float = mixed_rows.astype(jnp.float32)
    mean_square = jnp.mean(mixed_float * mixed_float, axis=-1, keepdims=True)
    normed = (mixed_float * lax.rsqrt(mean_square + 1e-05) * norm_gain).astype(jnp.bfloat16)
    token_count = clip_count * row_count
    top_count = routes.shape[-1]
    expert_count = lax.axis_size("exp") * gate_up_weight.shape[0]
    capacity = max(2, -(-(5 * token_count * top_count) // (4 * expert_count)))
    flat_routes = routes.reshape(-1)
    one_hot = (flat_routes[:, None] == jnp.arange(expert_count, dtype=jnp.int32)[None, :]).astype(
        jnp.int32
    )
    running_count = jnp.cumsum(one_hot, axis=0)
    slot_index = jnp.sum(running_count * one_hot, axis=1) - 1
    destination = flat_routes * capacity + slot_index
    slot_token = (
        jnp.zeros((expert_count * capacity,), jnp.int32)
        .at[destination]
        .set(jnp.arange(token_count * top_count, dtype=jnp.int32) // top_count)
    )
    normed, gate_up_far = lax.optimization_barrier((normed, gate_up_far))
    send_buffer = normed.reshape(token_count, feature_count)[slot_token]
    send_buffer = send_buffer.reshape(expert_count, capacity * 8, feature_count // 8)
    gate_up_blocks = near_blocks(gate_up_local, gate_up_far)
    down_blocks = near_blocks(down_local, down_far)
    portion = lax.all_to_all(send_buffer, "exp", split_axis=0, concat_axis=0, tiled=True)
    flattened = portion.reshape(-1, feature_count)
    summed = None
    for gate_up_block, down_block in zip(gate_up_blocks, down_blocks):
        gate_and_up = jnp.dot(flattened, gate_up_block, preferred_element_type=jnp.float32)
        hidden = (
            jax.nn.silu(gate_and_up[:, :local_units]) * gate_and_up[:, local_units:]
        ).astype(jnp.bfloat16)
        group_part = jnp.dot(hidden, down_block, preferred_element_type=jnp.float32)
        group_part = group_part.astype(jnp.bfloat16).astype(jnp.float32)
        summed = group_part if summed is None else summed + group_part
    summed = summed.astype(jnp.bfloat16).reshape(portion.shape)
    returned = lax.all_to_all(summed, "exp", split_axis=0, concat_axis=0, tiled=True)
    returned = returned.reshape(-1, feature_count)
    route_slots = destination.reshape(token_count, top_count)
    route_gates = gate_weights.reshape(token_count, top_count)
    expert_sum = None
    for route in range(top_count):
        term = route_gates[:, route : route + 1] * returned[route_slots[:, route]].astype(jnp.float32)
        expert_sum = term if expert_sum is None else expert_sum + term
    layer_out = (mixed_float.reshape(token_count, feature_count) + expert_sum).astype(jnp.bfloat16)
    return layer_out.reshape(clip_count, row_count, feature_count)


def solution(mesh):
    return jax.shard_map(
        shards,
        mesh=mesh,
        in_specs=(
            P("exp", "ctx", None),
            P("exp", "ctx", None),
            P("exp", "ctx", None),
            P("exp", "ctx", None),
            P(),
            P("exp", "ctx", None),
            P("exp", "ctx", None),
            P("exp", None, None, "ctx"),
            P("exp", "ctx", None),
        ),
        out_specs=P("exp", "ctx", None),
        check_vma=False,
    )
```

```python
import jax
import jax.numpy as jnp
from jax import lax
from jax.sharding import PartitionSpec as P

HEADS = 16


def far_block(block, after=None):
    if after is not None:
        block, _ = lax.optimization_barrier((block, after))
    return lax.ppermute(block, "ctx", perm=[(c, c ^ 2) for c in range(4)])


def near_blocks(block, far):
    perm = [(c, c ^ 1) for c in range(4)]
    return [block, far, lax.ppermute(block, "ctx", perm=perm), lax.ppermute(far, "ctx", perm=perm)]


def shards(
    queries,
    key_rows,
    value_rows,
    residual_in,
    norm_gain,
    routes,
    gate_weights,
    gate_up_weight,
    down_weight,
):
    clip_count, row_count, feature_count = queries.shape
    head_count = HEADS
    head_size = feature_count // head_count
    score_scale = head_size ** (-0.5)
    query_heads = queries.reshape(clip_count, row_count, head_count, head_size)
    running_max = jnp.full((clip_count, row_count, head_count), -1e30, jnp.float32)
    local_units = down_weight.shape[1]
    gate_up_local = gate_up_weight[0].reshape(feature_count, 2 * local_units)
    down_local = down_weight[0]
    key_far = far_block(key_rows)
    value_far = far_block(value_rows, key_far)
    gate_up_far = far_block(gate_up_local, value_far)
    down_far = far_block(down_local, gate_up_far)
    key_blocks = near_blocks(key_rows, key_far)
    value_blocks = near_blocks(value_rows, value_far)
    block_scores = [
        jnp.einsum(
            "cqhd,ckhd->cqhk",
            query_heads,
            block.reshape(clip_count, -1, head_count, head_size),
            preferred_element_type=jnp.float32,
        )
        * score_scale
        for block in key_blocks
    ]
    new_max = running_max
    for scores in block_scores:
        new_max = jnp.maximum(new_max, jnp.max(scores, axis=-1))
    running_sum = None
    weighted = None
    for scores, block in zip(block_scores, value_blocks):
        expo = jnp.exp(scores - new_max[..., None])
        block_sum = jnp.sum(expo, axis=-1)
        block_weighted = jnp.einsum(
            "cqhk,ckhd->cqhd",
            expo.astype(jnp.bfloat16),
            block.reshape(clip_count, -1, head_count, head_size),
            preferred_element_type=jnp.float32,
        )
        running_sum = block_sum if running_sum is None else running_sum + block_sum
        weighted = block_weighted if weighted is None else weighted + block_weighted
    final_max, final_sum = (new_max, running_sum)
    attention = (weighted / final_sum[..., None]).reshape(clip_count, row_count, feature_count)
    mixed_rows = (residual_in.astype(jnp.float32) + attention).astype(jnp.bfloat16)
    mixed_float = mixed_rows.astype(jnp.float32)
    mean_square = jnp.mean(mixed_float * mixed_float, axis=-1, keepdims=True)
    normed = (mixed_float * lax.rsqrt(mean_square + 1e-05) * norm_gain).astype(jnp.bfloat16)
    token_count = clip_count * row_count
    top_count = routes.shape[-1]
    expert_count = lax.axis_size("exp") * gate_up_weight.shape[0]
    capacity = max(2, -(-(5 * token_count * top_count) // (4 * expert_count)))
    flat_routes = routes.reshape(-1)
    one_hot = (flat_routes[:, None] == jnp.arange(expert_count, dtype=jnp.int32)[None, :]).astype(
        jnp.int32
    )
    running_count = jnp.cumsum(one_hot, axis=0)
    slot_index = jnp.sum(running_count * one_hot, axis=1) - 1
    destination = flat_routes * capacity + slot_index
    slot_token = (
        jnp.zeros((expert_count * capacity,), jnp.int32)
        .at[destination]
        .set(jnp.arange(token_count * top_count, dtype=jnp.int32) // top_count)
    )
    normed, gate_up_far = lax.optimization_barrier((normed, gate_up_far))
    send_buffer = normed.reshape(token_count, feature_count)[slot_token]
    send_buffer = send_buffer.reshape(expert_count, capacity * 8, feature_count // 8)
    gate_up_blocks = near_blocks(gate_up_local, gate_up_far)
    down_blocks = near_blocks(down_local, down_far)
    portion = lax.all_to_all(send_buffer, "exp", split_axis=0, concat_axis=0, tiled=True)
    flattened = portion.reshape(-1, feature_count)
    summed = None
    for gate_up_block, down_block in zip(gate_up_blocks, down_blocks):
        gate_and_up = jnp.dot(flattened, gate_up_block, preferred_element_type=jnp.float32)
        hidden = (
            jax.nn.silu(gate_and_up[:, :local_units]) * gate_and_up[:, local_units:]
        ).astype(jnp.bfloat16)
        group_part = jnp.dot(hidden, down_block, preferred_element_type=jnp.float32)
        group_part = group_part.astype(jnp.bfloat16).astype(jnp.float32)
        summed = group_part if summed is None else summed + group_part
    summed = summed.astype(jnp.bfloat16).reshape(portion.shape)
    returned = lax.all_to_all(summed, "exp", split_axis=0, concat_axis=0, tiled=True)
    returned = returned.reshape(-1, feature_count)
    route_slots = destination.reshape(token_count, top_count)
    route_gates = gate_weights.reshape(token_count, top_count)
    expert_sum = None
    for route in range(top_count):
        term = route_gates[:, route : route + 1] * returned[route_slots[:, route]].astype(jnp.float32)
        expert_sum = term if expert_sum is None else expert_sum + term
    layer_out = (mixed_float.reshape(token_count, feature_count) + expert_sum).astype(jnp.bfloat16)
    return layer_out.reshape(clip_count, row_count, feature_count)


def solution(mesh):
    return jax.shard_map(
        shards,
        mesh=mesh,
        in_specs=(
            P("exp", "ctx", None),
            P("exp", "ctx", None),
            P("exp", "ctx", None),
            P("exp", "ctx", None),
            P(),
            P("exp", "ctx", None),
            P("exp", "ctx", None),
            P("exp", None, None, "ctx"),
            P("exp", "ctx", None),
        ),
        out_specs=P("exp", "ctx", None),
        check_vma=False,
    )
```

```python
import jax
import jax.numpy as jnp
from jax import lax
from jax.sharding import PartitionSpec as P

HEADS = 16


def far_block(block, after=None):
    if after is not None:
        block, _ = lax.optimization_barrier((block, after))
    return lax.ppermute(block, "ctx", perm=[(c, c ^ 2) for c in range(4)])


def near_blocks(block, far):
    perm = [(c, c ^ 1) for c in range(4)]
    return [block, far, lax.ppermute(block, "ctx", perm=perm), lax.ppermute(far, "ctx", perm=perm)]


def shards(
    queries,
    key_rows,
    value_rows,
    residual_in,
    norm_gain,
    routes,
    gate_weights,
    gate_up_weight,
    down_weight,
):
    clip_count, row_count, feature_count = queries.shape
    head_count = HEADS
    head_size = feature_count // head_count
    score_scale = head_size ** (-0.5)
    query_heads = queries.reshape(clip_count, row_count, head_count, head_size)
    running_max = jnp.full((clip_count, row_count, head_count), -1e30, jnp.float32)
    local_units = down_weight.shape[1]
    gate_up_local = gate_up_weight[0].reshape(feature_count, 2 * local_units)
    down_local = down_weight[0]
    key_far = far_block(key_rows)
    value_far = far_block(value_rows, key_far)
    down_far = far_block(down_local, value_far)
    gate_up_far = far_block(gate_up_local, down_far)
    key_blocks = near_blocks(key_rows, key_far)
    value_blocks = near_blocks(value_rows, value_far)
    block_scores = [
        jnp.einsum(
            "cqhd,ckhd->cqhk",
            query_heads,
            block.reshape(clip_count, -1, head_count, head_size),
            preferred_element_type=jnp.float32,
        )
        * score_scale
        for block in key_blocks
    ]
    new_max = running_max
    for scores in block_scores:
        new_max = jnp.maximum(new_max, jnp.max(scores, axis=-1))
    running_sum = None
    weighted = None
    for scores, block in zip(block_scores, value_blocks):
        expo = jnp.exp(scores - new_max[..., None])
        block_sum = jnp.sum(expo, axis=-1)
        block_weighted = jnp.einsum(
            "cqhk,ckhd->cqhd",
            expo.astype(jnp.bfloat16),
            block.reshape(clip_count, -1, head_count, head_size),
            preferred_element_type=jnp.float32,
        )
        running_sum = block_sum if running_sum is None else running_sum + block_sum
        weighted = block_weighted if weighted is None else weighted + block_weighted
    final_max, final_sum = (new_max, running_sum)
    attention = (weighted / final_sum[..., None]).reshape(clip_count, row_count, feature_count)
    mixed_rows = (residual_in.astype(jnp.float32) + attention).astype(jnp.bfloat16)
    mixed_float = mixed_rows.astype(jnp.float32)
    mean_square = jnp.mean(mixed_float * mixed_float, axis=-1, keepdims=True)
    normed = (mixed_float * lax.rsqrt(mean_square + 1e-05) * norm_gain).astype(jnp.bfloat16)
    token_count = clip_count * row_count
    top_count = routes.shape[-1]
    expert_count = lax.axis_size("exp") * gate_up_weight.shape[0]
    capacity = max(2, -(-(5 * token_count * top_count) // (4 * expert_count)))
    flat_routes = routes.reshape(-1)
    one_hot = (flat_routes[:, None] == jnp.arange(expert_count, dtype=jnp.int32)[None, :]).astype(
        jnp.int32
    )
    running_count = jnp.cumsum(one_hot, axis=0)
    slot_index = jnp.sum(running_count * one_hot, axis=1) - 1
    destination = flat_routes * capacity + slot_index
    slot_token = (
        jnp.zeros((expert_count * capacity,), jnp.int32)
        .at[destination]
        .set(jnp.arange(token_count * top_count, dtype=jnp.int32) // top_count)
    )
    normed, down_far = lax.optimization_barrier((normed, down_far))
    send_buffer = normed.reshape(token_count, feature_count)[slot_token]
    send_buffer = send_buffer.reshape(expert_count, capacity * 8, feature_count // 8)
    gate_up_blocks = near_blocks(gate_up_local, gate_up_far)
    down_blocks = near_blocks(down_local, down_far)
    portion = lax.all_to_all(send_buffer, "exp", split_axis=0, concat_axis=0, tiled=True)
    flattened = portion.reshape(-1, feature_count)
    summed = None
    for gate_up_block, down_block in zip(gate_up_blocks, down_blocks):
        gate_and_up = jnp.dot(flattened, gate_up_block, preferred_element_type=jnp.float32)
        hidden = (
            jax.nn.silu(gate_and_up[:, :local_units]) * gate_and_up[:, local_units:]
        ).astype(jnp.bfloat16)
        group_part = jnp.dot(hidden, down_block, preferred_element_type=jnp.float32)
        group_part = group_part.astype(jnp.bfloat16).astype(jnp.float32)
        summed = group_part if summed is None else summed + group_part
    summed = summed.astype(jnp.bfloat16).reshape(portion.shape)
    returned = lax.all_to_all(summed, "exp", split_axis=0, concat_axis=0, tiled=True)
    returned = returned.reshape(-1, feature_count)
    route_slots = destination.reshape(token_count, top_count)
    route_gates = gate_weights.reshape(token_count, top_count)
    expert_sum = None
    for route in range(top_count):
        term = route_gates[:, route : route + 1] * returned[route_slots[:, route]].astype(jnp.float32)
        expert_sum = term if expert_sum is None else expert_sum + term
    layer_out = (mixed_float.reshape(token_count, feature_count) + expert_sum).astype(jnp.bfloat16)
    return layer_out.reshape(clip_count, row_count, feature_count)


def solution(mesh):
    return jax.shard_map(
        shards,
        mesh=mesh,
        in_specs=(
            P("exp", "ctx", None),
            P("exp", "ctx", None),
            P("exp", "ctx", None),
            P("exp", "ctx", None),
            P(),
            P("exp", "ctx", None),
            P("exp", "ctx", None),
            P("exp", None, None, "ctx"),
            P("exp", "ctx", None),
        ),
        out_specs=P("exp", "ctx", None),
        check_vma=False,
    )
```

```python
import jax
import jax.numpy as jnp
from jax import lax
from jax.sharding import PartitionSpec as P

HEADS = 16


def far_block(block, after=None):
    if after is not None:
        block, _ = lax.optimization_barrier((block, after))
    return lax.ppermute(block, "ctx", perm=[(c, c ^ 2) for c in range(4)])


def near_blocks(block, far):
    perm = [(c, c ^ 1) for c in range(4)]
    return [block, far, lax.ppermute(block, "ctx", perm=perm), lax.ppermute(far, "ctx", perm=perm)]


def shards(
    queries,
    key_rows,
    value_rows,
    residual_in,
    norm_gain,
    routes,
    gate_weights,
    gate_up_weight,
    down_weight,
):
    clip_count, row_count, feature_count = queries.shape
    head_count = HEADS
    head_size = feature_count // head_count
    score_scale = head_size ** (-0.5)
    query_heads = queries.reshape(clip_count, row_count, head_count, head_size)
    running_max = jnp.full((clip_count, row_count, head_count), -1e30, jnp.float32)
    local_units = down_weight.shape[1]
    gate_up_local = gate_up_weight[0].reshape(feature_count, 2 * local_units)
    down_local = down_weight[0]
    key_far = far_block(key_rows)
    value_far = far_block(value_rows, key_far)
    half_features = feature_count // 2
    half_units = local_units // 2
    gate_up_top = gate_up_local[:half_features]
    gate_up_bottom = gate_up_local[half_features:]
    down_top = down_local[:half_units]
    down_bottom = down_local[half_units:]
    gate_up_top_far = far_block(gate_up_top, value_far)
    down_top_far = far_block(down_top, gate_up_top_far)
    gate_up_bottom_far = far_block(gate_up_bottom, down_top_far)
    down_bottom_far = far_block(down_bottom, gate_up_bottom_far)
    key_blocks = near_blocks(key_rows, key_far)
    value_blocks = near_blocks(value_rows, value_far)
    block_scores = [
        jnp.einsum(
            "cqhd,ckhd->cqhk",
            query_heads,
            block.reshape(clip_count, -1, head_count, head_size),
            preferred_element_type=jnp.float32,
        )
        * score_scale
        for block in key_blocks
    ]
    new_max = running_max
    for scores in block_scores:
        new_max = jnp.maximum(new_max, jnp.max(scores, axis=-1))
    running_sum = None
    weighted = None
    for scores, block in zip(block_scores, value_blocks):
        expo = jnp.exp(scores - new_max[..., None])
        block_sum = jnp.sum(expo, axis=-1)
        block_weighted = jnp.einsum(
            "cqhk,ckhd->cqhd",
            expo.astype(jnp.bfloat16),
            block.reshape(clip_count, -1, head_count, head_size),
            preferred_element_type=jnp.float32,
        )
        running_sum = block_sum if running_sum is None else running_sum + block_sum
        weighted = block_weighted if weighted is None else weighted + block_weighted
    final_max, final_sum = (new_max, running_sum)
    attention = (weighted / final_sum[..., None]).reshape(clip_count, row_count, feature_count)
    mixed_rows = (residual_in.astype(jnp.float32) + attention).astype(jnp.bfloat16)
    mixed_float = mixed_rows.astype(jnp.float32)
    mean_square = jnp.mean(mixed_float * mixed_float, axis=-1, keepdims=True)
    normed = (mixed_float * lax.rsqrt(mean_square + 1e-05) * norm_gain).astype(jnp.bfloat16)
    token_count = clip_count * row_count
    top_count = routes.shape[-1]
    expert_count = lax.axis_size("exp") * gate_up_weight.shape[0]
    capacity = max(2, -(-(5 * token_count * top_count) // (4 * expert_count)))
    flat_routes = routes.reshape(-1)
    one_hot = (flat_routes[:, None] == jnp.arange(expert_count, dtype=jnp.int32)[None, :]).astype(
        jnp.int32
    )
    running_count = jnp.cumsum(one_hot, axis=0)
    slot_index = jnp.sum(running_count * one_hot, axis=1) - 1
    destination = flat_routes * capacity + slot_index
    slot_token = (
        jnp.zeros((expert_count * capacity,), jnp.int32)
        .at[destination]
        .set(jnp.arange(token_count * top_count, dtype=jnp.int32) // top_count)
    )
    normed, gate_up_top_far, down_top_far = lax.optimization_barrier(
        (normed, gate_up_top_far, down_top_far)
    )
    send_buffer = normed.reshape(token_count, feature_count)[slot_token]
    send_buffer = send_buffer.reshape(expert_count, capacity * 8, feature_count // 8)
    pieces = zip(
        near_blocks(gate_up_top, gate_up_top_far),
        near_blocks(gate_up_bottom, gate_up_bottom_far),
        near_blocks(down_top, down_top_far),
        near_blocks(down_bottom, down_bottom_far),
    )
    portion = lax.all_to_all(send_buffer, "exp", split_axis=0, concat_axis=0, tiled=True)
    flattened = portion.reshape(-1, feature_count)
    summed = None
    for top_block, bottom_block, down_top_block, down_bottom_block in pieces:
        gate_and_up = jnp.dot(
            flattened[:, :half_features], top_block, preferred_element_type=jnp.float32
        ) + jnp.dot(flattened[:, half_features:], bottom_block, preferred_element_type=jnp.float32)
        hidden = (
            jax.nn.silu(gate_and_up[:, :local_units]) * gate_and_up[:, local_units:]
        ).astype(jnp.bfloat16)
        group_part = jnp.dot(
            hidden[:, :half_units], down_top_block, preferred_element_type=jnp.float32
        ) + jnp.dot(hidden[:, half_units:], down_bottom_block, preferred_element_type=jnp.float32)
        group_part = group_part.astype(jnp.bfloat16).astype(jnp.float32)
        summed = group_part if summed is None else summed + group_part
    summed = summed.astype(jnp.bfloat16).reshape(portion.shape)
    returned = lax.all_to_all(summed, "exp", split_axis=0, concat_axis=0, tiled=True)
    returned = returned.reshape(-1, feature_count)
    route_slots = destination.reshape(token_count, top_count)
    route_gates = gate_weights.reshape(token_count, top_count)
    expert_sum = None
    for route in range(top_count):
        term = route_gates[:, route : route + 1] * returned[route_slots[:, route]].astype(jnp.float32)
        expert_sum = term if expert_sum is None else expert_sum + term
    layer_out = (mixed_float.reshape(token_count, feature_count) + expert_sum).astype(jnp.bfloat16)
    return layer_out.reshape(clip_count, row_count, feature_count)


def solution(mesh):
    return jax.shard_map(
        shards,
        mesh=mesh,
        in_specs=(
            P("exp", "ctx", None),
            P("exp", "ctx", None),
            P("exp", "ctx", None),
            P("exp", "ctx", None),
            P(),
            P("exp", "ctx", None),
            P("exp", "ctx", None),
            P("exp", None, None, "ctx"),
            P("exp", "ctx", None),
        ),
        out_specs=P("exp", "ctx", None),
        check_vma=False,
    )
```

```python
import jax
import jax.numpy as jnp
from jax import lax
from jax.sharding import PartitionSpec as P

HEADS = 16


def far_block(block, after=None):
    if after is not None:
        block, _ = lax.optimization_barrier((block, after))
    return lax.ppermute(block, "ctx", perm=[(c, c ^ 2) for c in range(4)])


def near_blocks(block, far):
    perm = [(c, c ^ 1) for c in range(4)]
    return [block, far, lax.ppermute(block, "ctx", perm=perm), lax.ppermute(far, "ctx", perm=perm)]


def shards(
    queries,
    key_rows,
    value_rows,
    residual_in,
    norm_gain,
    routes,
    gate_weights,
    gate_up_weight,
    down_weight,
):
    clip_count, row_count, feature_count = queries.shape
    head_count = HEADS
    head_size = feature_count // head_count
    score_scale = head_size ** (-0.5)
    query_heads = queries.reshape(clip_count, row_count, head_count, head_size)
    running_max = jnp.full((clip_count, row_count, head_count), -1e30, jnp.float32)
    local_units = down_weight.shape[1]
    gate_up_local = gate_up_weight[0].reshape(feature_count, 2 * local_units)
    down_local = down_weight[0]
    key_far = far_block(key_rows)
    value_far = far_block(value_rows, key_far)
    gate_up_far = far_block(gate_up_local, value_far)
    down_far = far_block(down_local, gate_up_far)
    key_blocks = near_blocks(key_rows, key_far)
    value_blocks = near_blocks(value_rows, value_far)
    block_scores = [
        jnp.einsum(
            "cqhd,ckhd->cqhk",
            query_heads,
            block.reshape(clip_count, -1, head_count, head_size),
            preferred_element_type=jnp.float32,
        )
        * score_scale
        for block in key_blocks
    ]
    new_max = running_max
    for scores in block_scores:
        new_max = jnp.maximum(new_max, jnp.max(scores, axis=-1))
    running_sum = None
    weighted = None
    for scores, block in zip(block_scores, value_blocks):
        expo = jnp.exp(scores - new_max[..., None])
        block_sum = jnp.sum(expo, axis=-1)
        block_weighted = jnp.einsum(
            "cqhk,ckhd->cqhd",
            expo.astype(jnp.bfloat16),
            block.reshape(clip_count, -1, head_count, head_size),
            preferred_element_type=jnp.float32,
        )
        running_sum = block_sum if running_sum is None else running_sum + block_sum
        weighted = block_weighted if weighted is None else weighted + block_weighted
    final_max, final_sum = (new_max, running_sum)
    attention = (weighted / final_sum[..., None]).reshape(clip_count, row_count, feature_count)
    mixed_rows = (residual_in.astype(jnp.float32) + attention).astype(jnp.bfloat16)
    mixed_float = mixed_rows.astype(jnp.float32)
    mean_square = jnp.mean(mixed_float * mixed_float, axis=-1, keepdims=True)
    normed = (mixed_float * lax.rsqrt(mean_square + 1e-05) * norm_gain).astype(jnp.bfloat16)
    token_count = clip_count * row_count
    top_count = routes.shape[-1]
    expert_count = lax.axis_size("exp") * gate_up_weight.shape[0]
    capacity = max(2, -(-(5 * token_count * top_count) // (4 * expert_count)))
    flat_routes = routes.reshape(-1)
    one_hot = (flat_routes[:, None] == jnp.arange(expert_count, dtype=jnp.int32)[None, :]).astype(
        jnp.int32
    )
    running_count = jnp.cumsum(one_hot, axis=0)
    slot_index = jnp.sum(running_count * one_hot, axis=1) - 1
    destination = flat_routes * capacity + slot_index
    slot_token = (
        jnp.zeros((expert_count * capacity,), jnp.int32)
        .at[destination]
        .set(jnp.arange(token_count * top_count, dtype=jnp.int32) // top_count)
    )
    send_buffer = normed.reshape(token_count, feature_count)[slot_token]
    send_buffer = send_buffer.reshape(expert_count, capacity * 8, feature_count // 8)
    send_buffer, gate_up_far = lax.optimization_barrier((send_buffer, gate_up_far))
    gate_up_blocks = near_blocks(gate_up_local, gate_up_far)
    down_blocks = near_blocks(down_local, down_far)
    portion = lax.all_to_all(send_buffer, "exp", split_axis=0, concat_axis=0, tiled=True)
    flattened = portion.reshape(-1, feature_count)
    summed = None
    for gate_up_block, down_block in zip(gate_up_blocks, down_blocks):
        gate_and_up = jnp.dot(flattened, gate_up_block, preferred_element_type=jnp.float32)
        hidden = (
            jax.nn.silu(gate_and_up[:, :local_units]) * gate_and_up[:, local_units:]
        ).astype(jnp.bfloat16)
        group_part = jnp.dot(hidden, down_block, preferred_element_type=jnp.float32)
        group_part = group_part.astype(jnp.bfloat16).astype(jnp.float32)
        summed = group_part if summed is None else summed + group_part
    summed = summed.astype(jnp.bfloat16).reshape(portion.shape)
    returned = lax.all_to_all(summed, "exp", split_axis=0, concat_axis=0, tiled=True)
    returned = returned.reshape(-1, feature_count)
    route_slots = destination.reshape(token_count, top_count)
    route_gates = gate_weights.reshape(token_count, top_count)
    expert_sum = None
    for route in range(top_count):
        term = route_gates[:, route : route + 1] * returned[route_slots[:, route]].astype(jnp.float32)
        expert_sum = term if expert_sum is None else expert_sum + term
    layer_out = (mixed_float.reshape(token_count, feature_count) + expert_sum).astype(jnp.bfloat16)
    return layer_out.reshape(clip_count, row_count, feature_count)


def solution(mesh):
    return jax.shard_map(
        shards,
        mesh=mesh,
        in_specs=(
            P("exp", "ctx", None),
            P("exp", "ctx", None),
            P("exp", "ctx", None),
            P("exp", "ctx", None),
            P(),
            P("exp", "ctx", None),
            P("exp", "ctx", None),
            P("exp", None, None, "ctx"),
            P("exp", "ctx", None),
        ),
        out_specs=P("exp", "ctx", None),
        check_vma=False,
    )
```

```python
import jax
import jax.numpy as jnp
from jax import lax
from jax.sharding import PartitionSpec as P

HEADS = 16


def far_block(block, after=None):
    if after is not None:
        block, _ = lax.optimization_barrier((block, after))
    return lax.ppermute(block, "ctx", perm=[(c, c ^ 2) for c in range(4)])


def near_blocks(block, far):
    perm = [(c, c ^ 1) for c in range(4)]
    return [block, far, lax.ppermute(block, "ctx", perm=perm), lax.ppermute(far, "ctx", perm=perm)]


def shards(
    queries,
    key_rows,
    value_rows,
    residual_in,
    norm_gain,
    routes,
    gate_weights,
    gate_up_weight,
    down_weight,
):
    clip_count, row_count, feature_count = queries.shape
    head_count = HEADS
    head_size = feature_count // head_count
    score_scale = head_size ** (-0.5)
    query_heads = queries.reshape(clip_count, row_count, head_count, head_size)
    running_max = jnp.full((clip_count, row_count, head_count), -1e30, jnp.float32)
    local_units = down_weight.shape[1]
    gate_up_local = gate_up_weight[0].reshape(feature_count, 2 * local_units)
    down_local = down_weight[0]
    key_far = far_block(key_rows)
    value_far = far_block(value_rows, key_far)
    gate_up_far = far_block(gate_up_local, value_far)
    down_far = far_block(down_local, gate_up_far)
    key_blocks = near_blocks(key_rows, key_far)
    value_blocks = near_blocks(value_rows, value_far)
    block_scores = [
        jnp.einsum(
            "cqhd,ckhd->cqhk",
            query_heads,
            block.reshape(clip_count, -1, head_count, head_size),
            preferred_element_type=jnp.float32,
        )
        * score_scale
        for block in key_blocks
    ]
    new_max = running_max
    for scores in block_scores:
        new_max = jnp.maximum(new_max, jnp.max(scores, axis=-1))
    running_sum = None
    weighted = None
    for scores, block in zip(block_scores, value_blocks):
        expo = jnp.exp(scores - new_max[..., None])
        block_sum = jnp.sum(expo, axis=-1)
        block_weighted = jnp.einsum(
            "cqhk,ckhd->cqhd",
            expo.astype(jnp.bfloat16),
            block.reshape(clip_count, -1, head_count, head_size),
            preferred_element_type=jnp.float32,
        )
        running_sum = block_sum if running_sum is None else running_sum + block_sum
        weighted = block_weighted if weighted is None else weighted + block_weighted
    final_max, final_sum = (new_max, running_sum)
    attention = (weighted / final_sum[..., None]).reshape(clip_count, row_count, feature_count)
    mixed_rows = (residual_in.astype(jnp.float32) + attention).astype(jnp.bfloat16)
    mixed_float = mixed_rows.astype(jnp.float32)
    mean_square = jnp.mean(mixed_float * mixed_float, axis=-1, keepdims=True)
    normed = (mixed_float * lax.rsqrt(mean_square + 1e-05) * norm_gain).astype(jnp.bfloat16)
    token_count = clip_count * row_count
    top_count = routes.shape[-1]
    expert_count = lax.axis_size("exp") * gate_up_weight.shape[0]
    capacity = max(2, -(-(5 * token_count * top_count) // (4 * expert_count)))
    flat_routes = routes.reshape(-1)
    one_hot = (flat_routes[:, None] == jnp.arange(expert_count, dtype=jnp.int32)[None, :]).astype(
        jnp.int32
    )
    running_count = jnp.cumsum(one_hot, axis=0)
    slot_index = jnp.sum(running_count * one_hot, axis=1) - 1
    destination = flat_routes * capacity + slot_index
    slot_token = (
        jnp.zeros((expert_count * capacity,), jnp.int32)
        .at[destination]
        .set(jnp.arange(token_count * top_count, dtype=jnp.int32) // top_count)
    )
    send_buffer = normed.reshape(token_count, feature_count)[slot_token]
    send_buffer = send_buffer.reshape(expert_count, capacity * 8, feature_count // 8)
    send_buffer, gate_up_far = lax.optimization_barrier((send_buffer, gate_up_far))
    gate_up_blocks = near_blocks(gate_up_local, gate_up_far)
    down_blocks = near_blocks(down_local, down_far)
    portion = lax.all_to_all(send_buffer, "exp", split_axis=0, concat_axis=0, tiled=True)
    flattened = portion.reshape(-1, feature_count)
    hiddens = []
    for gate_up_block in gate_up_blocks:
        gate_and_up = jnp.dot(flattened, gate_up_block, preferred_element_type=jnp.float32)
        hiddens.append(
            (jax.nn.silu(gate_and_up[:, :local_units]) * gate_and_up[:, local_units:]).astype(
                jnp.bfloat16
            )
        )
    route_slots = destination.reshape(token_count, top_count)
    route_gates = gate_weights.reshape(token_count, top_count)
    mixed_flat = mixed_float.reshape(token_count, feature_count)
    half_cols = feature_count // 2
    out_halves = []
    for half in range(2):
        cols = slice(half * half_cols, (half + 1) * half_cols)
        summed = None
        for hidden, down_block in zip(hiddens, down_blocks):
            group_part = jnp.dot(hidden, down_block[:, cols], preferred_element_type=jnp.float32)
            group_part = group_part.astype(jnp.bfloat16).astype(jnp.float32)
            summed = group_part if summed is None else summed + group_part
        summed = summed.astype(jnp.bfloat16).reshape(expert_count, capacity * 8, half_cols // 8)
        returned = lax.all_to_all(summed, "exp", split_axis=0, concat_axis=0, tiled=True)
        returned = returned.reshape(-1, half_cols)
        expert_sum = None
        for route in range(top_count):
            term = route_gates[:, route : route + 1] * returned[route_slots[:, route]].astype(
                jnp.float32
            )
            expert_sum = term if expert_sum is None else expert_sum + term
        out_halves.append((mixed_flat[:, cols] + expert_sum).astype(jnp.bfloat16))
    layer_out = jnp.concatenate(out_halves, axis=1)
    return layer_out.reshape(clip_count, row_count, feature_count)


def solution(mesh):
    return jax.shard_map(
        shards,
        mesh=mesh,
        in_specs=(
            P("exp", "ctx", None),
            P("exp", "ctx", None),
            P("exp", "ctx", None),
            P("exp", "ctx", None),
            P(),
            P("exp", "ctx", None),
            P("exp", "ctx", None),
            P("exp", None, None, "ctx"),
            P("exp", "ctx", None),
        ),
        out_specs=P("exp", "ctx", None),
        check_vma=False,
    )
```

```python
import jax
import jax.numpy as jnp
from jax import lax
from jax.sharding import PartitionSpec as P

HEADS = 16


def far_block(block, after=None):
    if after is not None:
        block, _ = lax.optimization_barrier((block, after))
    return lax.ppermute(block, "ctx", perm=[(c, c ^ 2) for c in range(4)])


def near_blocks(block, far):
    perm = [(c, c ^ 1) for c in range(4)]
    return [block, far, lax.ppermute(block, "ctx", perm=perm), lax.ppermute(far, "ctx", perm=perm)]


def shards(
    queries,
    key_rows,
    value_rows,
    residual_in,
    norm_gain,
    routes,
    gate_weights,
    gate_up_weight,
    down_weight,
):
    clip_count, row_count, feature_count = queries.shape
    head_count = HEADS
    head_size = feature_count // head_count
    score_scale = head_size ** (-0.5)
    query_heads = queries.reshape(clip_count, row_count, head_count, head_size)
    running_max = jnp.full((clip_count, row_count, head_count), -1e30, jnp.float32)
    local_units = down_weight.shape[1]
    gate_up_local = gate_up_weight[0].reshape(feature_count, 2 * local_units)
    down_local = down_weight[0]
    key_far = far_block(key_rows)
    value_far = far_block(value_rows, key_far)
    gate_up_far = far_block(gate_up_local, value_far)
    down_far = far_block(down_local, gate_up_far)
    key_blocks = near_blocks(key_rows, key_far)
    value_blocks = near_blocks(value_rows, value_far)
    block_scores = [
        jnp.einsum(
            "cqhd,ckhd->cqhk",
            query_heads,
            block.reshape(clip_count, -1, head_count, head_size),
            preferred_element_type=jnp.float32,
        )
        * score_scale
        for block in key_blocks
    ]
    new_max = running_max
    for scores in block_scores:
        new_max = jnp.maximum(new_max, jnp.max(scores, axis=-1))
    running_sum = None
    weighted = None
    for scores, block in zip(block_scores, value_blocks):
        expo = jnp.exp(scores - new_max[..., None])
        block_sum = jnp.sum(expo, axis=-1)
        block_weighted = jnp.einsum(
            "cqhk,ckhd->cqhd",
            expo.astype(jnp.bfloat16),
            block.reshape(clip_count, -1, head_count, head_size),
            preferred_element_type=jnp.float32,
        )
        running_sum = block_sum if running_sum is None else running_sum + block_sum
        weighted = block_weighted if weighted is None else weighted + block_weighted
    final_max, final_sum = (new_max, running_sum)
    attention = (weighted / final_sum[..., None]).reshape(clip_count, row_count, feature_count)
    mixed_rows = (residual_in.astype(jnp.float32) + attention).astype(jnp.bfloat16)
    mixed_float = mixed_rows.astype(jnp.float32)
    mean_square = jnp.mean(mixed_float * mixed_float, axis=-1, keepdims=True)
    normed = (mixed_float * lax.rsqrt(mean_square + 1e-05) * norm_gain).astype(jnp.bfloat16)
    token_count = clip_count * row_count
    top_count = routes.shape[-1]
    expert_count = lax.axis_size("exp") * gate_up_weight.shape[0]
    capacity = max(2, -(-(5 * token_count * top_count) // (4 * expert_count)))
    flat_routes = routes.reshape(-1)
    one_hot = (flat_routes[:, None] == jnp.arange(expert_count, dtype=jnp.int32)[None, :]).astype(
        jnp.int32
    )
    running_count = jnp.cumsum(one_hot, axis=0)
    slot_index = jnp.sum(running_count * one_hot, axis=1) - 1
    destination = flat_routes * capacity + slot_index
    slot_token = (
        jnp.zeros((expert_count * capacity,), jnp.int32)
        .at[destination]
        .set(jnp.arange(token_count * top_count, dtype=jnp.int32) // top_count)
    )
    send_buffer = normed.reshape(token_count, feature_count)[slot_token]
    send_buffer = send_buffer.reshape(expert_count, capacity * 8, feature_count // 8)
    send_buffer, gate_up_far = lax.optimization_barrier((send_buffer, gate_up_far))
    gate_up_blocks = near_blocks(gate_up_local, gate_up_far)
    down_blocks = near_blocks(down_local, down_far)
    portion = lax.all_to_all(send_buffer, "exp", split_axis=0, concat_axis=0, tiled=True)
    flattened = portion.reshape(-1, feature_count)
    block_count = len(gate_up_blocks)
    gate_and_up = jnp.dot(
        flattened, jnp.concatenate(gate_up_blocks, axis=1), preferred_element_type=jnp.float32
    ).reshape(-1, block_count, 2, local_units)
    hidden = (jax.nn.silu(gate_and_up[:, :, 0]) * gate_and_up[:, :, 1]).astype(jnp.bfloat16)
    summed = None
    for index, down_block in enumerate(down_blocks):
        group_part = jnp.dot(hidden[:, index], down_block, preferred_element_type=jnp.float32)
        group_part = group_part.astype(jnp.bfloat16).astype(jnp.float32)
        summed = group_part if summed is None else summed + group_part
    summed = summed.astype(jnp.bfloat16).reshape(portion.shape)
    returned = lax.all_to_all(summed, "exp", split_axis=0, concat_axis=0, tiled=True)
    returned = returned.reshape(-1, feature_count)
    route_slots = destination.reshape(token_count, top_count)
    route_gates = gate_weights.reshape(token_count, top_count)
    expert_sum = None
    for route in range(top_count):
        term = route_gates[:, route : route + 1] * returned[route_slots[:, route]].astype(jnp.float32)
        expert_sum = term if expert_sum is None else expert_sum + term
    layer_out = (mixed_float.reshape(token_count, feature_count) + expert_sum).astype(jnp.bfloat16)
    return layer_out.reshape(clip_count, row_count, feature_count)


def solution(mesh):
    return jax.shard_map(
        shards,
        mesh=mesh,
        in_specs=(
            P("exp", "ctx", None),
            P("exp", "ctx", None),
            P("exp", "ctx", None),
            P("exp", "ctx", None),
            P(),
            P("exp", "ctx", None),
            P("exp", "ctx", None),
            P("exp", None, None, "ctx"),
            P("exp", "ctx", None),
        ),
        out_specs=P("exp", "ctx", None),
        check_vma=False,
    )
```

```python
import jax
import jax.numpy as jnp
from jax import lax
from jax.sharding import PartitionSpec as P

HEADS = 16


def far_block(block, after=None):
    if after is not None:
        block, _ = lax.optimization_barrier((block, after))
    return lax.ppermute(block, "ctx", perm=[(c, c ^ 2) for c in range(4)])


def near_blocks(block, far):
    perm = [(c, c ^ 1) for c in range(4)]
    return [block, far, lax.ppermute(block, "ctx", perm=perm), lax.ppermute(far, "ctx", perm=perm)]


def shards(
    queries,
    key_rows,
    value_rows,
    residual_in,
    norm_gain,
    routes,
    gate_weights,
    gate_up_weight,
    down_weight,
):
    clip_count, row_count, feature_count = queries.shape
    head_count = HEADS
    head_size = feature_count // head_count
    score_scale = head_size ** (-0.5)
    query_heads = queries.reshape(clip_count, row_count, head_count, head_size)
    running_max = jnp.full((clip_count, row_count, head_count), -1e30, jnp.float32)
    local_units = down_weight.shape[1]
    gate_up_local = gate_up_weight[0].reshape(feature_count, 2 * local_units)
    down_local = down_weight[0]
    value_far = far_block(value_rows)
    key_far = far_block(key_rows, value_far)
    gate_up_far = far_block(gate_up_local, key_far)
    down_far = far_block(down_local, gate_up_far)
    key_blocks = near_blocks(key_rows, key_far)
    value_blocks = near_blocks(value_rows, value_far)
    block_scores = [
        jnp.einsum(
            "cqhd,ckhd->cqhk",
            query_heads,
            block.reshape(clip_count, -1, head_count, head_size),
            preferred_element_type=jnp.float32,
        )
        * score_scale
        for block in key_blocks
    ]
    new_max = running_max
    for scores in block_scores:
        new_max = jnp.maximum(new_max, jnp.max(scores, axis=-1))
    running_sum = None
    weighted = None
    for scores, block in zip(block_scores, value_blocks):
        expo = jnp.exp(scores - new_max[..., None])
        block_sum = jnp.sum(expo, axis=-1)
        block_weighted = jnp.einsum(
            "cqhk,ckhd->cqhd",
            expo.astype(jnp.bfloat16),
            block.reshape(clip_count, -1, head_count, head_size),
            preferred_element_type=jnp.float32,
        )
        running_sum = block_sum if running_sum is None else running_sum + block_sum
        weighted = block_weighted if weighted is None else weighted + block_weighted
    final_max, final_sum = (new_max, running_sum)
    attention = (weighted / final_sum[..., None]).reshape(clip_count, row_count, feature_count)
    mixed_rows = (residual_in.astype(jnp.float32) + attention).astype(jnp.bfloat16)
    mixed_float = mixed_rows.astype(jnp.float32)
    mean_square = jnp.mean(mixed_float * mixed_float, axis=-1, keepdims=True)
    normed = (mixed_float * lax.rsqrt(mean_square + 1e-05) * norm_gain).astype(jnp.bfloat16)
    token_count = clip_count * row_count
    top_count = routes.shape[-1]
    expert_count = lax.axis_size("exp") * gate_up_weight.shape[0]
    capacity = max(2, -(-(5 * token_count * top_count) // (4 * expert_count)))
    flat_routes = routes.reshape(-1)
    one_hot = (flat_routes[:, None] == jnp.arange(expert_count, dtype=jnp.int32)[None, :]).astype(
        jnp.int32
    )
    running_count = jnp.cumsum(one_hot, axis=0)
    slot_index = jnp.sum(running_count * one_hot, axis=1) - 1
    destination = flat_routes * capacity + slot_index
    slot_token = (
        jnp.zeros((expert_count * capacity,), jnp.int32)
        .at[destination]
        .set(jnp.arange(token_count * top_count, dtype=jnp.int32) // top_count)
    )
    send_buffer = normed.reshape(token_count, feature_count)[slot_token]
    send_buffer = send_buffer.reshape(expert_count, capacity * 8, feature_count // 8)
    send_buffer, gate_up_far = lax.optimization_barrier((send_buffer, gate_up_far))
    gate_up_blocks = near_blocks(gate_up_local, gate_up_far)
    down_blocks = near_blocks(down_local, down_far)
    portion = lax.all_to_all(send_buffer, "exp", split_axis=0, concat_axis=0, tiled=True)
    flattened = portion.reshape(-1, feature_count)
    summed = None
    for gate_up_block, down_block in zip(gate_up_blocks, down_blocks):
        gate_and_up = jnp.dot(flattened, gate_up_block, preferred_element_type=jnp.float32)
        hidden = (
            jax.nn.silu(gate_and_up[:, :local_units]) * gate_and_up[:, local_units:]
        ).astype(jnp.bfloat16)
        group_part = jnp.dot(hidden, down_block, preferred_element_type=jnp.float32)
        group_part = group_part.astype(jnp.bfloat16).astype(jnp.float32)
        summed = group_part if summed is None else summed + group_part
    summed = summed.astype(jnp.bfloat16).reshape(portion.shape)
    returned = lax.all_to_all(summed, "exp", split_axis=0, concat_axis=0, tiled=True)
    returned = returned.reshape(-1, feature_count)
    route_slots = destination.reshape(token_count, top_count)
    route_gates = gate_weights.reshape(token_count, top_count)
    expert_sum = None
    for route in range(top_count):
        term = route_gates[:, route : route + 1] * returned[route_slots[:, route]].astype(jnp.float32)
        expert_sum = term if expert_sum is None else expert_sum + term
    layer_out = (mixed_float.reshape(token_count, feature_count) + expert_sum).astype(jnp.bfloat16)
    return layer_out.reshape(clip_count, row_count, feature_count)


def solution(mesh):
    return jax.shard_map(
        shards,
        mesh=mesh,
        in_specs=(
            P("exp", "ctx", None),
            P("exp", "ctx", None),
            P("exp", "ctx", None),
            P("exp", "ctx", None),
            P(),
            P("exp", "ctx", None),
            P("exp", "ctx", None),
            P("exp", None, None, "ctx"),
            P("exp", "ctx", None),
        ),
        out_specs=P("exp", "ctx", None),
        check_vma=False,
    )
```

```python
import jax
import jax.numpy as jnp
from jax import lax
from jax.sharding import PartitionSpec as P

HEADS = 16


def far_block(block, after=None):
    if after is not None:
        block, _ = lax.optimization_barrier((block, after))
    return lax.ppermute(block, "ctx", perm=[(c, c ^ 2) for c in range(4)])


def near_blocks(block, far):
    perm = [(c, c ^ 1) for c in range(4)]
    return [block, far, lax.ppermute(block, "ctx", perm=perm), lax.ppermute(far, "ctx", perm=perm)]


def shards(
    queries,
    key_rows,
    value_rows,
    residual_in,
    norm_gain,
    routes,
    gate_weights,
    gate_up_weight,
    down_weight,
):
    clip_count, row_count, feature_count = queries.shape
    head_count = HEADS
    head_size = feature_count // head_count
    score_scale = head_size ** (-0.5)
    query_heads = queries.reshape(clip_count, row_count, head_count, head_size)
    running_max = jnp.full((clip_count, row_count, head_count), -1e30, jnp.float32)
    local_units = down_weight.shape[1]
    gate_up_local = gate_up_weight[0].reshape(feature_count, 2 * local_units)
    down_local = down_weight[0]
    key_far = far_block(key_rows)
    value_far = far_block(value_rows)
    gate_up_far = far_block(gate_up_local, value_far)
    down_far = far_block(down_local, gate_up_far)
    key_blocks = near_blocks(key_rows, key_far)
    value_blocks = near_blocks(value_rows, value_far)
    block_scores = [
        jnp.einsum(
            "cqhd,ckhd->cqhk",
            query_heads,
            block.reshape(clip_count, -1, head_count, head_size),
            preferred_element_type=jnp.float32,
        )
        * score_scale
        for block in key_blocks
    ]
    new_max = running_max
    for scores in block_scores:
        new_max = jnp.maximum(new_max, jnp.max(scores, axis=-1))
    running_sum = None
    weighted = None
    for scores, block in zip(block_scores, value_blocks):
        expo = jnp.exp(scores - new_max[..., None])
        block_sum = jnp.sum(expo, axis=-1)
        block_weighted = jnp.einsum(
            "cqhk,ckhd->cqhd",
            expo.astype(jnp.bfloat16),
            block.reshape(clip_count, -1, head_count, head_size),
            preferred_element_type=jnp.float32,
        )
        running_sum = block_sum if running_sum is None else running_sum + block_sum
        weighted = block_weighted if weighted is None else weighted + block_weighted
    final_max, final_sum = (new_max, running_sum)
    attention = (weighted / final_sum[..., None]).reshape(clip_count, row_count, feature_count)
    mixed_rows = (residual_in.astype(jnp.float32) + attention).astype(jnp.bfloat16)
    mixed_float = mixed_rows.astype(jnp.float32)
    mean_square = jnp.mean(mixed_float * mixed_float, axis=-1, keepdims=True)
    normed = (mixed_float * lax.rsqrt(mean_square + 1e-05) * norm_gain).astype(jnp.bfloat16)
    token_count = clip_count * row_count
    top_count = routes.shape[-1]
    expert_count = lax.axis_size("exp") * gate_up_weight.shape[0]
    capacity = max(2, -(-(5 * token_count * top_count) // (4 * expert_count)))
    flat_routes = routes.reshape(-1)
    one_hot = (flat_routes[:, None] == jnp.arange(expert_count, dtype=jnp.int32)[None, :]).astype(
        jnp.int32
    )
    running_count = jnp.cumsum(one_hot, axis=0)
    slot_index = jnp.sum(running_count * one_hot, axis=1) - 1
    destination = flat_routes * capacity + slot_index
    slot_token = (
        jnp.zeros((expert_count * capacity,), jnp.int32)
        .at[destination]
        .set(jnp.arange(token_count * top_count, dtype=jnp.int32) // top_count)
    )
    send_buffer = normed.reshape(token_count, feature_count)[slot_token]
    send_buffer = send_buffer.reshape(expert_count, capacity * 8, feature_count // 8)
    send_buffer, gate_up_far = lax.optimization_barrier((send_buffer, gate_up_far))
    gate_up_blocks = near_blocks(gate_up_local, gate_up_far)
    down_blocks = near_blocks(down_local, down_far)
    portion = lax.all_to_all(send_buffer, "exp", split_axis=0, concat_axis=0, tiled=True)
    flattened = portion.reshape(-1, feature_count)
    summed = None
    for gate_up_block, down_block in zip(gate_up_blocks, down_blocks):
        gate_and_up = jnp.dot(flattened, gate_up_block, preferred_element_type=jnp.float32)
        hidden = (
            jax.nn.silu(gate_and_up[:, :local_units]) * gate_and_up[:, local_units:]
        ).astype(jnp.bfloat16)
        group_part = jnp.dot(hidden, down_block, preferred_element_type=jnp.float32)
        group_part = group_part.astype(jnp.bfloat16).astype(jnp.float32)
        summed = group_part if summed is None else summed + group_part
    summed = summed.astype(jnp.bfloat16).reshape(portion.shape)
    returned = lax.all_to_all(summed, "exp", split_axis=0, concat_axis=0, tiled=True)
    returned = returned.reshape(-1, feature_count)
    route_slots = destination.reshape(token_count, top_count)
    route_gates = gate_weights.reshape(token_count, top_count)
    expert_sum = None
    for route in range(top_count):
        term = route_gates[:, route : route + 1] * returned[route_slots[:, route]].astype(jnp.float32)
        expert_sum = term if expert_sum is None else expert_sum + term
    layer_out = (mixed_float.reshape(token_count, feature_count) + expert_sum).astype(jnp.bfloat16)
    return layer_out.reshape(clip_count, row_count, feature_count)


def solution(mesh):
    return jax.shard_map(
        shards,
        mesh=mesh,
        in_specs=(
            P("exp", "ctx", None),
            P("exp", "ctx", None),
            P("exp", "ctx", None),
            P("exp", "ctx", None),
            P(),
            P("exp", "ctx", None),
            P("exp", "ctx", None),
            P("exp", None, None, "ctx"),
            P("exp", "ctx", None),
        ),
        out_specs=P("exp", "ctx", None),
        check_vma=False,
    )
```
